32 devices in a mesh: pair: 4 (over z), gen: 8 (over y, x, core).
Axes of the slice: x: 2, y: 2, z: 4, core: 2. Of those that a mesh axis runs over, the one named last changes fastest.
Arguments:
- tokens: bfloat16 [32768, 2048], P(('pair', 'gen')), may hold values from -6 to 6
- cotangent: bfloat16 [32768, 256], P(('pair', 'gen')), may hold values from -6 to 6
- block_pair: int32 [32, 1], replicated, may hold values from 0 to 15
- src_lang: int32 [16], replicated, may hold values from 0 to 95
- tgt_lang: int32 [16], replicated, may hold values from 0 to 95
- lang_embed: float32 [96, 512], P(None, 'pair'), may hold values from -5 to 5
- generator: bfloat16 [512, 524288], P('pair', 'gen'), may hold values from -0.005859375 to 0.005859375
Outputs:
- grad_tokens: bfloat16 [32768, 2048], P(('pair', 'gen'))
- grad_generator: bfloat16 [512, 524288], P('pair', 'gen')
- grad_embed: float32 [96, 512], P(None, 'pair')
The draws below stay inside these ranges and needn't reach their ends.
Inputs may be any that keep to these rules, and one draw needn't show every extreme that they name: `block_pair`: every pair owns at least one block; block counts per pair are uneven.
All inputs are finite; a program needn't handle non-finite values.
Results may differ from the reference program's by a relative error of at most 0.007.
Values may be sent and summed in bfloat16 or wider, within the bound.
No kernel may reach another device: no remote copies, remote signals or barrier semaphores. Data moves between devices by JAX's collectives and lax.ppermute only.
A program may use at most 128 MiB of HBM per device.

```python
import jax
import jax.numpy as jnp
from jax import lax

E = 512
D = 2048
R = 256
LANGS = 96
PAIRS = 16
BLK = 1024
BLOCKS = 32
TOKENS = 32768


def plant(values, stream_key, least, largest):
    extent = values.shape
    place = [jax.random.randint(jax.random.fold_in(stream_key, axis), (), 0, extent[axis]) for axis in range(len(extent))]
    values = values.at[tuple(place)].set(least)
    longest = extent.index(max(extent))
    place[longest] = (place[longest] + 1) % extent[longest]
    return values.at[tuple(place)].set(largest)


def levels(key, shape, cuts, low, largest):
    gain, own = 1.0, jax.random.fold_in(key, 6)
    for axis_at, parts in cuts:
        draws = jnp.exp(jax.random.uniform(jax.random.fold_in(own, axis_at), (parts,), jnp.float32, low / len(cuts), largest / len(cuts)))
        gain = gain * jnp.repeat(draws, shape[axis_at] // parts).reshape([-1 if axis == axis_at else 1 for axis in range(len(shape))])
    return gain


def different_ones(own_key, rows, count, top, lift):
    ranking = jax.random.permutation(jax.random.fold_in(own_key, 1), count)
    pull = ranking
    for power in range(3):
        pull = pull * pull // count
    pull = pull * lift // count
    lots = jax.random.randint(jax.random.fold_in(own_key, 2), (rows, count), 0, 4096) + pull
    sure = jax.random.permutation(jax.random.fold_in(own_key, 3), rows)[jnp.arange(count) % rows]
    lots = jnp.where(jnp.arange(rows)[:, None] == sure[None, :], 1 << 14, lots)
    merit = lots * count + jnp.arange(count)
    return lax.top_k(merit.astype(jnp.int32), top)[1].astype(jnp.int32)


def noise(stream_key, extent, width, limit, cuts=(), kind=jnp.bfloat16):
    level = levels(stream_key, extent, cuts, -0.22, 0.18) if cuts else 1.0
    entries = jax.random.normal(stream_key, extent, jnp.float32) * width * level
    return jnp.minimum(jnp.maximum(entries, -limit), limit).astype(kind)


def setup_inputs(seed: int = 0) -> dict:
    key_list = jax.random.split(jax.random.key(seed), 8)
    return {
        "tokens": noise(key_list[0], (TOKENS, D), 1.0, 6.0, ((0, 32),)),
        "cotangent": noise(key_list[1], (TOKENS, R), 1.0, 6.0, ((0, 32),)),
        "block_pair": different_ones(key_list[2], BLOCKS, PAIRS, 1, 1024),
        "src_lang": plant(jax.random.randint(key_list[3], (PAIRS,), 0, LANGS), jax.random.fold_in(key_list[3], 1), 0, LANGS - 1).astype(jnp.int32),
        "tgt_lang": plant(jax.random.randint(key_list[4], (PAIRS,), 0, LANGS), jax.random.fold_in(key_list[4], 1), 0, LANGS - 1).astype(jnp.int32),
        "lang_embed": noise(key_list[5], (LANGS, E), 0.7, 5.0, ((1, 4),), jnp.float32),
        "generator": noise(key_list[6], (E, D * R), (E * D) ** -0.5, 0.005859375, ((0, 4), (1, 8))),
    }


def reference(tokens, cotangent, block_pair, src_lang, tgt_lang, lang_embed, generator):
    src_rows = jnp.take(lang_embed, src_lang, axis=0)
    tgt_rows = jnp.take(lang_embed, tgt_lang, axis=0)
    pair_embed = (src_rows + tgt_rows).astype(jnp.bfloat16)
    adapters = jnp.dot(pair_embed, generator, preferred_element_type=jnp.float32).astype(jnp.bfloat16)
    token_blocks = tokens.reshape(BLOCKS, BLK, D)
    cot_blocks = cotangent.reshape(BLOCKS, BLK, R)

    def block_step(running, inputs):
        x_block, cot_block, pair_id = inputs
        adapter = lax.dynamic_index_in_dim(adapters, pair_id, 0, keepdims=False).reshape(D, R)
        hidden = jnp.dot(x_block, adapter, preferred_element_type=jnp.float32)
        logistic = jax.nn.sigmoid(hidden)
        grad_hidden = (cot_block.astype(jnp.float32) * logistic * (1.0 + hidden * (1.0 - logistic))).astype(jnp.bfloat16)
        grad_block = jnp.dot(grad_hidden, adapter.T, preferred_element_type=jnp.float32).astype(jnp.bfloat16)
        outer_grad = jnp.dot(x_block.T, grad_hidden, preferred_element_type=jnp.float32).reshape(D * R)
        running = running.at[pair_id].add(outer_grad)
        return running, grad_block

    start_grads = jnp.zeros((PAIRS, D * R), jnp.float32)
    grad_adapters, grad_blocks = lax.scan(block_step, start_grads, (token_blocks, cot_blocks, block_pair[:, 0]))
    grad_rounded = grad_adapters.astype(jnp.bfloat16)
    grad_generator = jnp.dot(pair_embed.T, grad_rounded, preferred_element_type=jnp.float32).astype(jnp.bfloat16)
    grad_pair = jnp.dot(grad_rounded, generator.T, preferred_element_type=jnp.float32)
    grad_embed = jnp.zeros((LANGS, E), jnp.float32).at[src_lang].add(grad_pair).at[tgt_lang].add(grad_pair)
    return grad_blocks.reshape(TOKENS, D), grad_generator, grad_embed
```

```python
import jax
import jax.numpy as jnp
from jax import lax
from jax.sharding import PartitionSpec as P

BLK = 1024


def shards(tokens, cotangent, block_pair, src_lang, tgt_lang, lang_embed, generator):
    gen_count = lax.axis_size("gen")
    pair_count_axis = lax.axis_size("pair")
    blocks_here = tokens.shape[0] // BLK
    model_width = tokens.shape[1]
    adapter_rank = cotangent.shape[1]
    languages = lang_embed.shape[0]
    pair_count = src_lang.shape[0]
    chunk = generator.shape[1]
    quarter = chunk // pair_count_axis
    lang_ids = jnp.arange(languages, dtype=jnp.int32)
    hot_both = (src_lang[:, None] == lang_ids[None, :]).astype(jnp.float32) + (
        tgt_lang[:, None] == lang_ids[None, :]
    ).astype(jnp.float32)
    pair_embed = jnp.dot(hot_both, lang_embed, precision=lax.Precision.HIGHEST).astype(jnp.bfloat16)
    partial_value = jnp.dot(pair_embed, generator, preferred_element_type=jnp.float32)
    adapter_part = lax.psum_scatter(
        partial_value, "pair", scatter_dimension=1, tiled=True
    ).astype(jnp.bfloat16)
    flat_pairs = block_pair[:, 0]
    outgoing = jnp.take(adapter_part, flat_pairs, axis=0)
    incoming = lax.all_to_all(outgoing, ("pair", "gen"), 0, 0, tiled=True)
    adapters = (
        incoming.reshape(pair_count_axis, gen_count, quarter)
        .transpose(1, 0, 2)
        .reshape(blocks_here, model_width, adapter_rank)
    )
    token_blocks = tokens.reshape(blocks_here, BLK, model_width)
    cot_blocks = cotangent.reshape(blocks_here, BLK, adapter_rank)
    hidden = jnp.einsum("btd,bdr->btr", token_blocks, adapters, preferred_element_type=jnp.float32)
    logistic = jax.nn.sigmoid(hidden)
    grad_hidden = (
        cot_blocks.astype(jnp.float32) * logistic * (1.0 + hidden * (1.0 - logistic))
    ).astype(jnp.bfloat16)
    grad_tokens = (
        jnp.einsum("btr,bdr->btd", grad_hidden, adapters, preferred_element_type=jnp.float32)
        .astype(jnp.bfloat16)
        .reshape(tokens.shape)
    )
    outer_grads = jnp.einsum(
        "btd,btr->bdr", token_blocks, grad_hidden, preferred_element_type=jnp.float32
    )
    by_owner = (
        outer_grads.reshape(gen_count, pair_count_axis, quarter)
        .transpose(1, 0, 2)
        .reshape(pair_count_axis * gen_count, quarter)
    )
    returned = lax.all_to_all(by_owner, ("pair", "gen"), 0, 0, tiled=True)
    pair_ids = jnp.arange(pair_count, dtype=jnp.int32)
    segment_hot = (pair_ids[:, None] == flat_pairs[None, :]).astype(jnp.float32)
    row_grad = jnp.dot(segment_hot, returned, precision=lax.Precision.HIGHEST).astype(jnp.bfloat16)
    grad_rounded = lax.all_gather(row_grad, "pair", axis=1, tiled=True)
    grad_generator = jnp.einsum(
        "pe,pc->ec", pair_embed, grad_rounded, preferred_element_type=jnp.float32
    ).astype(jnp.bfloat16)
    partial_pair = jnp.einsum(
        "pc,ec->pe", grad_rounded, generator, preferred_element_type=jnp.float32
    )
    grad_pair = lax.psum(partial_pair, "gen")
    grad_embed = jnp.dot(hot_both.T, grad_pair, precision=lax.Precision.HIGHEST)
    return (grad_tokens, grad_generator, grad_embed)


def solution(mesh):
    placed = (
        P(("pair", "gen"), None),
        P(("pair", "gen"), None),
        P(),
        P(),
        P(),
        P(None, "pair"),
        P("pair", "gen"),
    )
    return jax.shard_map(
        shards,
        mesh=mesh,
        in_specs=placed,
        out_specs=(P(("pair", "gen"), None), P("pair", "gen"), P(None, "pair")),
        check_vma=False,
    )
```

```python
import jax
import jax.numpy as jnp
from jax import lax
from jax.sharding import PartitionSpec as P

BLK = 1024


def shards(tokens, cotangent, block_pair, src_lang, tgt_lang, lang_embed, generator):
    gen_count = lax.axis_size("gen")
    pair_count_axis = lax.axis_size("pair")
    blocks_here = tokens.shape[0] // BLK
    model_width = tokens.shape[1]
    adapter_rank = cotangent.shape[1]
    languages = lang_embed.shape[0]
    pair_count = src_lang.shape[0]
    chunk = generator.shape[1]
    quarter = chunk // pair_count_axis
    lang_ids = jnp.arange(languages, dtype=jnp.int32)
    hot_both = (src_lang[:, None] == lang_ids[None, :]).astype(jnp.float32) + (
        tgt_lang[:, None] == lang_ids[None, :]
    ).astype(jnp.float32)
    pair_embed = jnp.dot(hot_both, lang_embed, precision=lax.Precision.HIGHEST).astype(jnp.bfloat16)
    partial_value = jnp.dot(pair_embed, generator, preferred_element_type=jnp.float32)
    adapter_part = lax.psum_scatter(
        partial_value.astype(jnp.bfloat16), "pair", scatter_dimension=1, tiled=True
    )
    flat_pairs = block_pair[:, 0]
    outgoing = jnp.take(adapter_part, flat_pairs, axis=0)
    incoming = lax.all_to_all(outgoing, ("pair", "gen"), 0, 0, tiled=True)
    adapters = (
        incoming.reshape(pair_count_axis, gen_count, quarter)
        .transpose(1, 0, 2)
        .reshape(blocks_here, model_width, adapter_rank)
    )
    token_blocks = tokens.reshape(blocks_here, BLK, model_width)
    cot_blocks = cotangent.reshape(blocks_here, BLK, adapter_rank)
    hidden = jnp.einsum("btd,bdr->btr", token_blocks, adapters, preferred_element_type=jnp.float32)
    logistic = jax.nn.sigmoid(hidden)
    grad_hidden = (
        cot_blocks.astype(jnp.float32) * logistic * (1.0 + hidden * (1.0 - logistic))
    ).astype(jnp.bfloat16)
    grad_tokens = (
        jnp.einsum("btr,bdr->btd", grad_hidden, adapters, preferred_element_type=jnp.float32)
        .astype(jnp.bfloat16)
        .reshape(tokens.shape)
    )
    outer_grads = jnp.einsum(
        "btd,btr->bdr", token_blocks, grad_hidden, preferred_element_type=jnp.float32
    )
    by_owner = (
        outer_grads.reshape(gen_count, pair_count_axis, quarter)
        .transpose(1, 0, 2)
        .reshape(pair_count_axis * gen_count, quarter)
        .astype(jnp.bfloat16)
    )
    returned = lax.all_to_all(by_owner, ("pair", "gen"), 0, 0, tiled=True)
    pair_ids = jnp.arange(pair_count, dtype=jnp.int32)
    segment_hot = (pair_ids[:, None] == flat_pairs[None, :]).astype(jnp.float32)
    row_grad = jnp.dot(segment_hot, returned.astype(jnp.float32), precision=lax.Precision.HIGHEST).astype(jnp.bfloat16)
    grad_rounded = lax.all_gather(row_grad, "pair", axis=1, tiled=True)
    grad_generator = jnp.einsum(
        "pe,pc->ec", pair_embed, grad_rounded, preferred_element_type=jnp.float32
    ).astype(jnp.bfloat16)
    partial_pair = jnp.einsum(
        "pc,ec->pe", grad_rounded, generator, preferred_element_type=jnp.float32
    )
    grad_pair = lax.psum(partial_pair, "gen")
    grad_embed = jnp.dot(hot_both.T, grad_pair, precision=lax.Precision.HIGHEST)
    return (grad_tokens, grad_generator, grad_embed)


def solution(mesh):
    placed = (
        P(("pair", "gen"), None),
        P(("pair", "gen"), None),
        P(),
        P(),
        P(),
        P(None, "pair"),
        P("pair", "gen"),
    )
    return jax.shard_map(
        shards,
        mesh=mesh,
        in_specs=placed,
        out_specs=(P(("pair", "gen"), None), P("pair", "gen"), P(None, "pair")),
        check_vma=False,
    )
```

```python
import jax
import jax.numpy as jnp
from jax import lax
from jax.sharding import PartitionSpec as P

BLK = 1024


def shards(tokens, cotangent, block_pair, src_lang, tgt_lang, lang_embed, generator):
    gen_count = lax.axis_size("gen")
    pair_count_axis = lax.axis_size("pair")
    blocks_here = tokens.shape[0] // BLK
    model_width = tokens.shape[1]
    adapter_rank = cotangent.shape[1]
    languages = lang_embed.shape[0]
    pair_count = src_lang.shape[0]
    chunk = generator.shape[1]
    quarter = chunk // pair_count_axis
    lang_ids = jnp.arange(languages, dtype=jnp.int32)
    hot_both = (src_lang[:, None] == lang_ids[None, :]).astype(jnp.float32) + (
        tgt_lang[:, None] == lang_ids[None, :]
    ).astype(jnp.float32)
    pair_embed = jnp.dot(hot_both, lang_embed, precision=lax.Precision.HIGHEST).astype(jnp.bfloat16)
    partial_value = jnp.dot(pair_embed, generator, preferred_element_type=jnp.float32)
    adapter_part = lax.psum_scatter(
        partial_value, "pair", scatter_dimension=1, tiled=True
    ).astype(jnp.bfloat16)
    flat_pairs = block_pair[:, 0]
    outgoing = jnp.take(adapter_part, flat_pairs, axis=0)
    incoming = lax.all_to_all(outgoing, ("pair", "gen"), 0, 0, tiled=True)
    adapters = (
        incoming.reshape(pair_count_axis, gen_count, quarter)
        .transpose(1, 0, 2)
        .reshape(blocks_here, model_width, adapter_rank)
    )
    token_blocks = tokens.reshape(blocks_here, BLK, model_width)
    cot_blocks = cotangent.reshape(blocks_here, BLK, adapter_rank)
    hidden = jnp.einsum("btd,bdr->btr", token_blocks, adapters, preferred_element_type=jnp.float32)
    logistic = jax.nn.sigmoid(hidden)
    grad_hidden = (
        cot_blocks.astype(jnp.float32) * logistic * (1.0 + hidden * (1.0 - logistic))
    ).astype(jnp.bfloat16)
    grad_tokens = (
        jnp.einsum("btr,bdr->btd", grad_hidden, adapters, preferred_element_type=jnp.float32)
        .astype(jnp.bfloat16)
        .reshape(tokens.shape)
    )
    outer_grads = jnp.einsum(
        "btd,btr->bdr", token_blocks, grad_hidden, preferred_element_type=jnp.float32
    )
    by_owner = (
        outer_grads.reshape(gen_count, pair_count_axis, quarter)
        .transpose(1, 0, 2)
        .reshape(pair_count_axis * gen_count, quarter)
        .astype(jnp.bfloat16)
    )
    returned = lax.all_to_all(by_owner, ("pair", "gen"), 0, 0, tiled=True)
    pair_ids = jnp.arange(pair_count, dtype=jnp.int32)
    segment_hot = (pair_ids[:, None] == flat_pairs[None, :]).astype(jnp.float32)
    row_grad = jnp.dot(segment_hot, returned.astype(jnp.float32), precision=lax.Precision.HIGHEST).astype(jnp.bfloat16)
    grad_rounded = lax.all_gather(row_grad, "pair", axis=1, tiled=True)
    grad_generator = jnp.einsum(
        "pe,pc->ec", pair_embed, grad_rounded, preferred_element_type=jnp.float32
    ).astype(jnp.bfloat16)
    partial_pair = jnp.einsum(
        "pc,ec->pe", grad_rounded, generator, preferred_element_type=jnp.float32
    )
    grad_pair = lax.psum(partial_pair, "gen")
    grad_embed = jnp.dot(hot_both.T, grad_pair, precision=lax.Precision.HIGHEST)
    return (grad_tokens, grad_generator, grad_embed)


def solution(mesh):
    placed = (
        P(("pair", "gen"), None),
        P(("pair", "gen"), None),
        P(),
        P(),
        P(),
        P(None, "pair"),
        P("pair", "gen"),
    )
    return jax.shard_map(
        shards,
        mesh=mesh,
        in_specs=placed,
        out_specs=(P(("pair", "gen"), None), P("pair", "gen"), P(None, "pair")),
        check_vma=False,
    )
```

```python
import jax
import jax.numpy as jnp
from jax import lax
from jax.sharding import PartitionSpec as P

BLK = 1024


def shards(tokens, cotangent, block_pair, src_lang, tgt_lang, lang_embed, generator):
    gen_count = lax.axis_size("gen")
    pair_count_axis = lax.axis_size("pair")
    blocks_here = tokens.shape[0] // BLK
    model_width = tokens.shape[1]
    adapter_rank = cotangent.shape[1]
    languages = lang_embed.shape[0]
    pair_count = src_lang.shape[0]
    chunk = generator.shape[1]
    quarter = chunk // pair_count_axis
    lang_ids = jnp.arange(languages, dtype=jnp.int32)
    hot_both = (src_lang[:, None] == lang_ids[None, :]).astype(jnp.float32) + (
        tgt_lang[:, None] == lang_ids[None, :]
    ).astype(jnp.float32)
    pair_embed = jnp.dot(hot_both, lang_embed, precision=lax.Precision.HIGHEST).astype(jnp.bfloat16)
    partial_value = jnp.dot(pair_embed, generator, preferred_element_type=jnp.float32)
    adapter_part = lax.psum_scatter(
        partial_value, "pair", scatter_dimension=1, tiled=True
    ).astype(jnp.bfloat16)
    flat_pairs = block_pair[:, 0]
    gen_major_pairs = flat_pairs.reshape(pair_count_axis, gen_count).T.reshape(-1)
    outgoing = jnp.take(adapter_part, gen_major_pairs, axis=0)
    incoming = lax.all_to_all(outgoing, ("gen", "pair"), 0, 0, tiled=True)
    adapters = incoming.reshape(blocks_here, model_width, adapter_rank)
    token_blocks = tokens.reshape(blocks_here, BLK, model_width)
    cot_blocks = cotangent.reshape(blocks_here, BLK, adapter_rank)
    hidden = jnp.einsum("btd,bdr->btr", token_blocks, adapters, preferred_element_type=jnp.float32)
    logistic = jax.nn.sigmoid(hidden)
    grad_hidden = (
        cot_blocks.astype(jnp.float32) * logistic * (1.0 + hidden * (1.0 - logistic))
    ).astype(jnp.bfloat16)
    grad_tokens = (
        jnp.einsum("btr,bdr->btd", grad_hidden, adapters, preferred_element_type=jnp.float32)
        .astype(jnp.bfloat16)
        .reshape(tokens.shape)
    )
    outer_grads = jnp.einsum(
        "btd,btr->bdr", token_blocks, grad_hidden, preferred_element_type=jnp.float32
    )
    by_owner = outer_grads.reshape(gen_count * pair_count_axis, quarter).astype(jnp.bfloat16)
    returned = lax.all_to_all(by_owner, ("gen", "pair"), 0, 0, tiled=True)
    pair_ids = jnp.arange(pair_count, dtype=jnp.int32)
    segment_hot = (pair_ids[:, None] == gen_major_pairs[None, :]).astype(jnp.float32)
    row_grad = jnp.dot(segment_hot, returned.astype(jnp.float32), precision=lax.Precision.HIGHEST).astype(jnp.bfloat16)
    grad_rounded = lax.all_gather(row_grad, "pair", axis=1, tiled=True)
    grad_generator = jnp.einsum(
        "pe,pc->ec", pair_embed, grad_rounded, preferred_element_type=jnp.float32
    ).astype(jnp.bfloat16)
    partial_pair = jnp.einsum(
        "pc,ec->pe", grad_rounded, generator, preferred_element_type=jnp.float32
    )
    grad_pair = partial_pair
    span = 1
    while span < gen_count:
        swap = [(i, i ^ span) for i in range(gen_count)]
        grad_pair = grad_pair + lax.ppermute(grad_pair, "gen", swap)
        span *= 2
    grad_embed = jnp.dot(hot_both.T, grad_pair, precision=lax.Precision.HIGHEST)
    return (grad_tokens, grad_generator, grad_embed)


def solution(mesh):
    placed = (
        P(("pair", "gen"), None),
        P(("pair", "gen"), None),
        P(),
        P(),
        P(),
        P(None, "pair"),
        P("pair", "gen"),
    )
    return jax.shard_map(
        shards,
        mesh=mesh,
        in_specs=placed,
        out_specs=(P(("pair", "gen"), None), P("pair", "gen"), P(None, "pair")),
        check_vma=False,
    )
```

```python
import jax
import jax.numpy as jnp
from jax import lax
from jax.sharding import PartitionSpec as P

BLK = 1024


def shards(tokens, cotangent, block_pair, src_lang, tgt_lang, lang_embed, generator):
    gen_count = lax.axis_size("gen")
    pair_count_axis = lax.axis_size("pair")
    blocks_here = tokens.shape[0] // BLK
    model_width = tokens.shape[1]
    adapter_rank = cotangent.shape[1]
    languages = lang_embed.shape[0]
    pair_count = src_lang.shape[0]
    chunk = generator.shape[1]
    quarter = chunk // pair_count_axis
    lang_ids = jnp.arange(languages, dtype=jnp.int32)
    hot_both = (src_lang[:, None] == lang_ids[None, :]).astype(jnp.float32) + (
        tgt_lang[:, None] == lang_ids[None, :]
    ).astype(jnp.float32)
    pair_embed = jnp.dot(hot_both, lang_embed, precision=lax.Precision.HIGHEST).astype(jnp.bfloat16)
    partial_value = jnp.dot(pair_embed, generator, preferred_element_type=jnp.float32)
    adapter_part = lax.psum_scatter(
        partial_value, "pair", scatter_dimension=1, tiled=True
    ).astype(jnp.bfloat16)
    flat_pairs = block_pair[:, 0]
    gen_major_pairs = flat_pairs.reshape(pair_count_axis, gen_count).T.reshape(-1)
    rows_per = quarter // adapter_rank
    outgoing = jnp.take(adapter_part.reshape(pair_count, rows_per, adapter_rank), gen_major_pairs, axis=0)
    incoming = lax.all_to_all(outgoing, ("gen", "pair"), 0, 0, tiled=True)
    adapters = incoming.reshape(blocks_here, model_width, adapter_rank)
    token_blocks = tokens.reshape(blocks_here, BLK, model_width)
    cot_blocks = cotangent.reshape(blocks_here, BLK, adapter_rank)
    hidden = jnp.einsum("btd,bdr->btr", token_blocks, adapters, preferred_element_type=jnp.float32)
    logistic = jax.nn.sigmoid(hidden)
    grad_hidden = (
        cot_blocks.astype(jnp.float32) * logistic * (1.0 + hidden * (1.0 - logistic))
    ).astype(jnp.bfloat16)
    grad_tokens = (
        jnp.einsum("btr,bdr->btd", grad_hidden, adapters, preferred_element_type=jnp.float32)
        .astype(jnp.bfloat16)
        .reshape(tokens.shape)
    )
    outer_grads = jnp.einsum(
        "btd,btr->bdr", token_blocks, grad_hidden, preferred_element_type=jnp.float32
    )
    by_owner = outer_grads.reshape(gen_count * pair_count_axis, rows_per, adapter_rank).astype(jnp.bfloat16)
    returned = lax.all_to_all(by_owner, ("gen", "pair"), 0, 0, tiled=True)
    pair_ids = jnp.arange(pair_count, dtype=jnp.int32)
    segment_hot = (pair_ids[:, None] == gen_major_pairs[None, :]).astype(jnp.float32)
    row_grad = (
        jnp.einsum("pb,bxr->pxr", segment_hot, returned.astype(jnp.float32), precision=lax.Precision.HIGHEST)
        .astype(jnp.bfloat16)
        .reshape(pair_count, quarter)
    )
    grad_rounded = lax.all_gather(row_grad, "pair", axis=1, tiled=True)
    grad_generator = jnp.einsum(
        "pe,pc->ec", pair_embed, grad_rounded, preferred_element_type=jnp.float32
    ).astype(jnp.bfloat16)
    partial_pair = jnp.einsum(
        "pc,ec->pe", grad_rounded, generator, preferred_element_type=jnp.float32
    )
    grad_pair = partial_pair
    span = 1
    while span < gen_count:
        swap = [(i, i ^ span) for i in range(gen_count)]
        grad_pair = grad_pair + lax.ppermute(grad_pair, "gen", swap)
        span *= 2
    grad_embed = jnp.dot(hot_both.T, grad_pair, precision=lax.Precision.HIGHEST)
    return (grad_tokens, grad_generator, grad_embed)


def solution(mesh):
    placed = (
        P(("pair", "gen"), None),
        P(("pair", "gen"), None),
        P(),
        P(),
        P(),
        P(None, "pair"),
        P("pair", "gen"),
    )
    return jax.shard_map(
        shards,
        mesh=mesh,
        in_specs=placed,
        out_specs=(P(("pair", "gen"), None), P("pair", "gen"), P(None, "pair")),
        check_vma=False,
    )
```

```python
import jax
import jax.numpy as jnp
from jax import lax
from jax.sharding import PartitionSpec as P

BLK = 1024


def shards(tokens, cotangent, block_pair, src_lang, tgt_lang, lang_embed, generator):
    gen_count = lax.axis_size("gen")
    pair_count_axis = lax.axis_size("pair")
    blocks_here = tokens.shape[0] // BLK
    model_width = tokens.shape[1]
    adapter_rank = cotangent.shape[1]
    languages = lang_embed.shape[0]
    pair_count = src_lang.shape[0]
    chunk = generator.shape[1]
    quarter = chunk // pair_count_axis
    lang_ids = jnp.arange(languages, dtype=jnp.int32)
    hot_both = (src_lang[:, None] == lang_ids[None, :]).astype(jnp.float32) + (
        tgt_lang[:, None] == lang_ids[None, :]
    ).astype(jnp.float32)
    pair_embed = jnp.dot(hot_both, lang_embed, precision=lax.Precision.HIGHEST).astype(jnp.bfloat16)
    partial_value = jnp.dot(pair_embed, generator, preferred_element_type=jnp.float32)
    adapter_part = lax.psum_scatter(
        partial_value, "pair", scatter_dimension=1, tiled=True
    ).astype(jnp.bfloat16)
    flat_pairs = block_pair[:, 0]
    gen_major_pairs = flat_pairs.reshape(pair_count_axis, gen_count).T.reshape(-1)
    rows_per = quarter // adapter_rank
    outgoing = jnp.take(adapter_part.reshape(pair_count, rows_per, adapter_rank), gen_major_pairs, axis=0)
    incoming = lax.all_to_all(outgoing, ("gen", "pair"), 0, 0, tiled=True)
    adapters = incoming.reshape(blocks_here, model_width, adapter_rank)
    token_blocks = tokens.reshape(blocks_here, BLK, model_width)
    cot_blocks = cotangent.reshape(blocks_here, BLK, adapter_rank)
    hidden = jnp.einsum("btd,bdr->btr", token_blocks, adapters, preferred_element_type=jnp.float32)
    logistic = jax.nn.sigmoid(hidden)
    grad_hidden = (
        cot_blocks.astype(jnp.float32) * logistic * (1.0 + hidden * (1.0 - logistic))
    ).astype(jnp.bfloat16)
    grad_tokens = (
        jnp.einsum("btr,bdr->btd", grad_hidden, adapters, preferred_element_type=jnp.float32)
        .astype(jnp.bfloat16)
        .reshape(tokens.shape)
    )
    outer_grads = jnp.einsum(
        "btd,btr->bdr", token_blocks, grad_hidden, preferred_element_type=jnp.float32
    )
    halves = 2
    slice_rows = rows_per // halves
    by_owner = (
        outer_grads.reshape(gen_count, halves, pair_count_axis, slice_rows, adapter_rank)
        .transpose(0, 2, 1, 3, 4)
        .reshape(gen_count * pair_count_axis, rows_per, adapter_rank)
        .astype(jnp.bfloat16)
    )
    returned = lax.all_to_all(by_owner, ("gen", "pair"), 0, 0, tiled=True)
    pair_ids = jnp.arange(pair_count, dtype=jnp.int32)
    segment_hot = (pair_ids[:, None] == gen_major_pairs[None, :]).astype(jnp.float32)
    row_grad = (
        jnp.einsum("pb,bxr->pxr", segment_hot, returned.astype(jnp.float32), precision=lax.Precision.HIGHEST)
        .astype(jnp.bfloat16)
        .reshape(pair_count, halves, slice_rows * adapter_rank)
    )
    half_cols = chunk // halves
    grad_halves = []
    partial_pair = None
    for h in range(halves):
        grad_half = lax.all_gather(row_grad[:, h], "pair", axis=1, tiled=True)
        grad_halves.append(grad_half)
        part = jnp.einsum(
            "pc,ec->pe", grad_half, generator[:, h * half_cols:(h + 1) * half_cols],
            preferred_element_type=jnp.float32,
        )
        partial_pair = part if partial_pair is None else partial_pair + part
    grad_rounded = jnp.concatenate(grad_halves, axis=1)
    grad_generator = jnp.einsum(
        "pe,pc->ec", pair_embed, grad_rounded, preferred_element_type=jnp.float32
    ).astype(jnp.bfloat16)
    grad_pair = partial_pair
    span = 1
    while span < gen_count:
        swap = [(i, i ^ span) for i in range(gen_count)]
        grad_pair = grad_pair + lax.ppermute(grad_pair, "gen", swap)
        span *= 2
    grad_embed = jnp.dot(hot_both.T, grad_pair, precision=lax.Precision.HIGHEST)
    return (grad_tokens, grad_generator, grad_embed)


def solution(mesh):
    placed = (
        P(("pair", "gen"), None),
        P(("pair", "gen"), None),
        P(),
        P(),
        P(),
        P(None, "pair"),
        P("pair", "gen"),
    )
    return jax.shard_map(
        shards,
        mesh=mesh,
        in_specs=placed,
        out_specs=(P(("pair", "gen"), None), P("pair", "gen"), P(None, "pair")),
        check_vma=False,
    )
```

```python
import jax
import jax.numpy as jnp
from jax import lax
from jax.sharding import PartitionSpec as P
from jax.experimental import pallas as pl
from jax.experimental.pallas import tpu as pltpu

BLK = 1024
TAIL_COLS = 4096


def _tail_kernel(embed_t_ref, grad_ref, gen_ref, out_ref, pair_ref):
    step = pl.program_id(0)
    grad_tile = grad_ref[...]
    out_ref[...] = jnp.dot(
        embed_t_ref[...], grad_tile, preferred_element_type=jnp.float32
    ).astype(out_ref.dtype)
    part = lax.dot_general(
        grad_tile, gen_ref[...], (((1,), (1,)), ((), ())), preferred_element_type=jnp.float32
    )

    @pl.when(step == 0)
    def _():
        pair_ref[...] = part

    @pl.when(step > 0)
    def _():
        pair_ref[...] += part


def grad_tail(embed_t, grad_rounded, generator):
    feats, cols = generator.shape
    pairs = grad_rounded.shape[0]
    tile = min(TAIL_COLS, cols)
    return pl.pallas_call(
        _tail_kernel,
        grid=(cols // tile,),
        in_specs=[
            pl.BlockSpec((feats, pairs), lambda i: (0, 0)),
            pl.BlockSpec((pairs, tile), lambda i: (0, i)),
            pl.BlockSpec((feats, tile), lambda i: (0, i)),
        ],
        out_specs=[
            pl.BlockSpec((feats, tile), lambda i: (0, i)),
            pl.BlockSpec((pairs, feats), lambda i: (0, 0)),
        ],
        out_shape=[
            jax.ShapeDtypeStruct((feats, cols), jnp.bfloat16),
            jax.ShapeDtypeStruct((pairs, feats), jnp.float32),
        ],
        compiler_params=pltpu.CompilerParams(dimension_semantics=("arbitrary",)),
        cost_estimate=pl.CostEstimate(
            flops=4 * feats * cols * pairs,
            transcendentals=0,
            bytes_accessed=2 * (2 * feats * cols + pairs * cols),
        ),
    )(embed_t, grad_rounded, generator)


def shards(tokens, cotangent, block_pair, src_lang, tgt_lang, lang_embed, generator):
    gen_count = lax.axis_size("gen")
    pair_count_axis = lax.axis_size("pair")
    blocks_here = tokens.shape[0] // BLK
    model_width = tokens.shape[1]
    adapter_rank = cotangent.shape[1]
    languages = lang_embed.shape[0]
    pair_count = src_lang.shape[0]
    chunk = generator.shape[1]
    quarter = chunk // pair_count_axis
    lang_ids = jnp.arange(languages, dtype=jnp.int32)
    hot_both = (src_lang[:, None] == lang_ids[None, :]).astype(jnp.float32) + (
        tgt_lang[:, None] == lang_ids[None, :]
    ).astype(jnp.float32)
    pair_embed = jnp.dot(hot_both, lang_embed, precision=lax.Precision.HIGHEST).astype(jnp.bfloat16)
    partial_value = jnp.dot(pair_embed, generator, preferred_element_type=jnp.float32)
    adapter_part = lax.psum_scatter(
        partial_value, "pair", scatter_dimension=1, tiled=True
    ).astype(jnp.bfloat16)
    flat_pairs = block_pair[:, 0]
    gen_major_pairs = flat_pairs.reshape(pair_count_axis, gen_count).T.reshape(-1)
    rows_per = quarter // adapter_rank
    outgoing = jnp.take(adapter_part.reshape(pair_count, rows_per, adapter_rank), gen_major_pairs, axis=0)
    incoming = lax.all_to_all(outgoing, ("gen", "pair"), 0, 0, tiled=True)
    adapters = incoming.reshape(blocks_here, model_width, adapter_rank)
    token_blocks = tokens.reshape(blocks_here, BLK, model_width)
    cot_blocks = cotangent.reshape(blocks_here, BLK, adapter_rank)
    hidden = jnp.einsum("btd,bdr->btr", token_blocks, adapters, preferred_element_type=jnp.float32)
    logistic = jax.nn.sigmoid(hidden)
    grad_hidden = (
        cot_blocks.astype(jnp.float32) * logistic * (1.0 + hidden * (1.0 - logistic))
    ).astype(jnp.bfloat16)
    grad_tokens = (
        jnp.einsum("btr,bdr->btd", grad_hidden, adapters, preferred_element_type=jnp.float32)
        .astype(jnp.bfloat16)
        .reshape(tokens.shape)
    )
    outer_grads = jnp.einsum(
        "btd,btr->bdr", token_blocks, grad_hidden, preferred_element_type=jnp.float32
    )
    by_owner = outer_grads.reshape(gen_count * pair_count_axis, rows_per, adapter_rank).astype(jnp.bfloat16)
    returned = lax.all_to_all(by_owner, ("gen", "pair"), 0, 0, tiled=True)
    pair_ids = jnp.arange(pair_count, dtype=jnp.int32)
    segment_hot = (pair_ids[:, None] == gen_major_pairs[None, :]).astype(jnp.float32)
    row_grad = (
        jnp.einsum("pb,bxr->pxr", segment_hot, returned.astype(jnp.float32), precision=lax.Precision.HIGHEST)
        .astype(jnp.bfloat16)
        .reshape(pair_count, quarter)
    )
    grad_rounded = lax.all_gather(row_grad, "pair", axis=1, tiled=True)
    grad_generator, partial_pair = grad_tail(pair_embed.T, grad_rounded, generator)
    grad_pair = partial_pair
    span = 1
    while span < gen_count:
        swap = [(i, i ^ span) for i in range(gen_count)]
        grad_pair = grad_pair + lax.ppermute(grad_pair, "gen", swap)
        span *= 2
    grad_embed = jnp.dot(hot_both.T, grad_pair, precision=lax.Precision.HIGHEST)
    return (grad_tokens, grad_generator, grad_embed)


def solution(mesh):
    placed = (
        P(("pair", "gen"), None),
        P(("pair", "gen"), None),
        P(),
        P(),
        P(),
        P(None, "pair"),
        P("pair", "gen"),
    )
    return jax.shard_map(
        shards,
        mesh=mesh,
        in_specs=placed,
        out_specs=(P(("pair", "gen"), None), P("pair", "gen"), P(None, "pair")),
        check_vma=False,
    )
```

```python
import jax
import jax.numpy as jnp
from jax import lax
from jax.sharding import PartitionSpec as P
from jax.experimental import pallas as pl
from jax.experimental.pallas import tpu as pltpu

BLK = 1024
TAIL_COLS = 8192


def _tail_kernel(embed_t_ref, grad_ref, gen_ref, out_ref, pair_ref):
    step = pl.program_id(0)
    grad_tile = grad_ref[...]
    out_ref[...] = jnp.dot(
        embed_t_ref[...], grad_tile, preferred_element_type=jnp.float32
    ).astype(out_ref.dtype)
    part = lax.dot_general(
        gen_ref[...], grad_tile, (((1,), (1,)), ((), ())), preferred_element_type=jnp.float32
    )

    @pl.when(step == 0)
    def _():
        pair_ref[...] = part

    @pl.when(step > 0)
    def _():
        pair_ref[...] += part


def grad_tail(embed_t, grad_rounded, generator):
    feats, cols = generator.shape
    pairs = grad_rounded.shape[0]
    tile = min(TAIL_COLS, cols)
    return pl.pallas_call(
        _tail_kernel,
        grid=(cols // tile,),
        in_specs=[
            pl.BlockSpec((feats, pairs), lambda i: (0, 0)),
            pl.BlockSpec((pairs, tile), lambda i: (0, i)),
            pl.BlockSpec((feats, tile), lambda i: (0, i)),
        ],
        out_specs=[
            pl.BlockSpec((feats, tile), lambda i: (0, i)),
            pl.BlockSpec((feats, pairs), lambda i: (0, 0)),
        ],
        out_shape=[
            jax.ShapeDtypeStruct((feats, cols), jnp.bfloat16),
            jax.ShapeDtypeStruct((feats, pairs), jnp.float32),
        ],
        compiler_params=pltpu.CompilerParams(dimension_semantics=("arbitrary",)),
        cost_estimate=pl.CostEstimate(
            flops=4 * feats * cols * pairs,
            transcendentals=0,
            bytes_accessed=2 * (2 * feats * cols + pairs * cols),
        ),
    )(embed_t, grad_rounded, generator)


def shards(tokens, cotangent, block_pair, src_lang, tgt_lang, lang_embed, generator):
    gen_count = lax.axis_size("gen")
    pair_count_axis = lax.axis_size("pair")
    blocks_here = tokens.shape[0] // BLK
    model_width = tokens.shape[1]
    adapter_rank = cotangent.shape[1]
    languages = lang_embed.shape[0]
    pair_count = src_lang.shape[0]
    chunk = generator.shape[1]
    quarter = chunk // pair_count_axis
    lang_ids = jnp.arange(languages, dtype=jnp.int32)
    hot_both = (src_lang[:, None] == lang_ids[None, :]).astype(jnp.float32) + (
        tgt_lang[:, None] == lang_ids[None, :]
    ).astype(jnp.float32)
    pair_embed = jnp.dot(hot_both, lang_embed, precision=lax.Precision.HIGHEST).astype(jnp.bfloat16)
    partial_value = jnp.dot(pair_embed, generator, preferred_element_type=jnp.float32)
    adapter_part = lax.psum_scatter(
        partial_value, "pair", scatter_dimension=1, tiled=True
    ).astype(jnp.bfloat16)
    flat_pairs = block_pair[:, 0]
    gen_major_pairs = flat_pairs.reshape(pair_count_axis, gen_count).T.reshape(-1)
    rows_per = quarter // adapter_rank
    outgoing = jnp.take(adapter_part.reshape(pair_count, rows_per, adapter_rank), gen_major_pairs, axis=0)
    incoming = lax.all_to_all(outgoing, ("gen", "pair"), 0, 0, tiled=True)
    adapters = incoming.reshape(blocks_here, model_width, adapter_rank)
    token_blocks = tokens.reshape(blocks_here, BLK, model_width)
    cot_blocks = cotangent.reshape(blocks_here, BLK, adapter_rank)
    hidden = jnp.einsum("btd,bdr->btr", token_blocks, adapters, preferred_element_type=jnp.float32)
    logistic = jax.nn.sigmoid(hidden)
    grad_hidden = (
        cot_blocks.astype(jnp.float32) * logistic * (1.0 + hidden * (1.0 - logistic))
    ).astype(jnp.bfloat16)
    grad_tokens = (
        jnp.einsum("btr,bdr->btd", grad_hidden, adapters, preferred_element_type=jnp.float32)
        .astype(jnp.bfloat16)
        .reshape(tokens.shape)
    )
    outer_grads = jnp.einsum(
        "btd,btr->bdr", token_blocks, grad_hidden, preferred_element_type=jnp.float32
    )
    by_owner = outer_grads.reshape(gen_count * pair_count_axis, rows_per, adapter_rank).astype(jnp.bfloat16)
    returned = lax.all_to_all(by_owner, ("gen", "pair"), 0, 0, tiled=True)
    pair_ids = jnp.arange(pair_count, dtype=jnp.int32)
    segment_hot = (pair_ids[:, None] == gen_major_pairs[None, :]).astype(jnp.float32)
    row_grad = (
        jnp.einsum("pb,bxr->pxr", segment_hot, returned.astype(jnp.float32), precision=lax.Precision.HIGHEST)
        .astype(jnp.bfloat16)
        .reshape(pair_count, quarter)
    )
    grad_rounded = lax.all_gather(row_grad, "pair", axis=1, tiled=True)
    grad_generator, pair_part_t = grad_tail(pair_embed.T, grad_rounded, generator)
    partial_pair = pair_part_t.T
    grad_pair = partial_pair
    span = 1
    while span < gen_count:
        swap = [(i, i ^ span) for i in range(gen_count)]
        grad_pair = grad_pair + lax.ppermute(grad_pair, "gen", swap)
        span *= 2
    grad_embed = jnp.dot(hot_both.T, grad_pair, precision=lax.Precision.HIGHEST)
    return (grad_tokens, grad_generator, grad_embed)


def solution(mesh):
    placed = (
        P(("pair", "gen"), None),
        P(("pair", "gen"), None),
        P(),
        P(),
        P(),
        P(None, "pair"),
        P("pair", "gen"),
    )
    return jax.shard_map(
        shards,
        mesh=mesh,
        in_specs=placed,
        out_specs=(P(("pair", "gen"), None), P("pair", "gen"), P(None, "pair")),
        check_vma=False,
    )
```

```python
import jax
import jax.numpy as jnp
from jax import lax
from jax.sharding import PartitionSpec as P
from jax.experimental import pallas as pl
from jax.experimental.pallas import tpu as pltpu

BLK = 1024
TAIL_COLS = 8192


def _tail_kernel(embed_t_ref, grad_ref, gen_ref, out_ref, pair_ref):
    step = pl.program_id(0)
    grad_tile = grad_ref[...]
    out_ref[...] = jnp.dot(
        embed_t_ref[...], grad_tile, preferred_element_type=jnp.float32
    ).astype(out_ref.dtype)
    part = lax.dot_general(
        gen_ref[...], grad_tile, (((1,), (1,)), ((), ())), preferred_element_type=jnp.float32
    )

    @pl.when(step == 0)
    def _():
        pair_ref[...] = part

    @pl.when(step > 0)
    def _():
        pair_ref[...] += part


def grad_tail(embed_t, grad_rounded, generator):
    feats, cols = generator.shape
    pairs = grad_rounded.shape[0]
    tile = min(TAIL_COLS, cols)
    return pl.pallas_call(
        _tail_kernel,
        grid=(cols // tile,),
        in_specs=[
            pl.BlockSpec((feats, pairs), lambda i: (0, 0)),
            pl.BlockSpec((pairs, tile), lambda i: (0, i)),
            pl.BlockSpec((feats, tile), lambda i: (0, i)),
        ],
        out_specs=[
            pl.BlockSpec((feats, tile), lambda i: (0, i)),
            pl.BlockSpec((feats, pairs), lambda i: (0, 0)),
        ],
        out_shape=[
            jax.ShapeDtypeStruct((feats, cols), jnp.bfloat16),
            jax.ShapeDtypeStruct((feats, pairs), jnp.float32),
        ],
        compiler_params=pltpu.CompilerParams(dimension_semantics=("arbitrary",)),
        cost_estimate=pl.CostEstimate(
            flops=4 * feats * cols * pairs,
            transcendentals=0,
            bytes_accessed=2 * (2 * feats * cols + pairs * cols),
        ),
    )(embed_t, grad_rounded, generator)


def shards(tokens, cotangent, block_pair, src_lang, tgt_lang, lang_embed, generator):
    gen_count = lax.axis_size("gen")
    pair_count_axis = lax.axis_size("pair")
    blocks_here = tokens.shape[0] // BLK
    model_width = tokens.shape[1]
    adapter_rank = cotangent.shape[1]
    languages = lang_embed.shape[0]
    pair_count = src_lang.shape[0]
    chunk = generator.shape[1]
    quarter = chunk // pair_count_axis
    lang_ids = jnp.arange(languages, dtype=jnp.int32)
    hot_both = (src_lang[:, None] == lang_ids[None, :]).astype(jnp.float32) + (
        tgt_lang[:, None] == lang_ids[None, :]
    ).astype(jnp.float32)
    pair_embed = jnp.dot(hot_both, lang_embed, precision=lax.Precision.HIGHEST).astype(jnp.bfloat16)
    partial_value = jnp.dot(pair_embed, generator, preferred_element_type=jnp.float32)
    adapter_part = lax.psum_scatter(
        partial_value, "pair", scatter_dimension=1, tiled=True
    ).astype(jnp.bfloat16)
    flat_pairs = block_pair[:, 0]
    gen_major_pairs = flat_pairs.reshape(pair_count_axis, gen_count).T.reshape(-1)
    rows_per = quarter // adapter_rank
    outgoing = jnp.take(adapter_part.reshape(pair_count, rows_per, adapter_rank), gen_major_pairs, axis=0)
    incoming = lax.all_to_all(outgoing, ("gen", "pair"), 0, 0, tiled=True)
    adapters = incoming.reshape(blocks_here, model_width, adapter_rank)
    token_blocks = tokens.reshape(blocks_here, BLK, model_width)
    cot_blocks = cotangent.reshape(blocks_here, BLK, adapter_rank)
    hidden = jnp.einsum("btd,bdr->btr", token_blocks, adapters, preferred_element_type=jnp.float32)
    logistic = jax.nn.sigmoid(hidden)
    grad_hidden = (
        cot_blocks.astype(jnp.float32) * logistic * (1.0 + hidden * (1.0 - logistic))
    ).astype(jnp.bfloat16)
    grad_tokens = (
        jnp.einsum("btr,bdr->btd", grad_hidden, adapters, preferred_element_type=jnp.float32)
        .astype(jnp.bfloat16)
        .reshape(tokens.shape)
    )
    outer_grads = jnp.einsum(
        "btd,btr->bdr", token_blocks, grad_hidden, preferred_element_type=jnp.float32
    )
    by_owner = outer_grads.reshape(gen_count * pair_count_axis, rows_per, adapter_rank).astype(jnp.bfloat16)
    returned = lax.all_to_all(by_owner, ("gen", "pair"), 0, 0, tiled=True)
    pair_ids = jnp.arange(pair_count, dtype=jnp.int32)
    segment_hot = (pair_ids[:, None] == gen_major_pairs[None, :]).astype(jnp.float32)
    row_grad = (
        jnp.einsum("pb,bxr->pxr", segment_hot, returned.astype(jnp.float32), precision=lax.Precision.HIGHEST)
        .astype(jnp.bfloat16)
        .reshape(pair_count, quarter)
    )
    grad_rounded = lax.all_gather(row_grad, "pair", axis=1, tiled=True)
    grad_generator, pair_part_t = grad_tail(pair_embed.T, grad_rounded, generator)
    partial_pair = pair_part_t.T
    grad_pair = partial_pair
    if gen_count <= 8:
        for shift in range(1, gen_count):
            ring = [(i, (i + shift) % gen_count) for i in range(gen_count)]
            grad_pair = grad_pair + lax.ppermute(partial_pair, "gen", ring)
    else:
        span = 1
        while span < gen_count:
            swap = [(i, i ^ span) for i in range(gen_count)]
            grad_pair = grad_pair + lax.ppermute(grad_pair, "gen", swap)
            span *= 2
    grad_embed = jnp.dot(hot_both.T, grad_pair, precision=lax.Precision.HIGHEST)
    return (grad_tokens, grad_generator, grad_embed)


def solution(mesh):
    placed = (
        P(("pair", "gen"), None),
        P(("pair", "gen"), None),
        P(),
        P(),
        P(),
        P(None, "pair"),
        P("pair", "gen"),
    )
    return jax.shard_map(
        shards,
        mesh=mesh,
        in_specs=placed,
        out_specs=(P(("pair", "gen"), None), P("pair", "gen"), P(None, "pair")),
        check_vma=False,
    )
```

```python
import jax
import jax.numpy as jnp
from jax import lax
from jax.sharding import PartitionSpec as P

BLK = 1024


def shards(tokens, cotangent, block_pair, src_lang, tgt_lang, lang_embed, generator):
    gen_count = lax.axis_size("gen")
    pair_count_axis = lax.axis_size("pair")
    blocks_here = tokens.shape[0] // BLK
    model_width = tokens.shape[1]
    adapter_rank = cotangent.shape[1]
    languages = lang_embed.shape[0]
    pair_count = src_lang.shape[0]
    chunk = generator.shape[1]
    quarter = chunk // pair_count_axis
    lang_ids = jnp.arange(languages, dtype=jnp.int32)
    hot_both = (src_lang[:, None] == lang_ids[None, :]).astype(jnp.float32) + (
        tgt_lang[:, None] == lang_ids[None, :]
    ).astype(jnp.float32)
    pair_embed = jnp.dot(hot_both, lang_embed, precision=lax.Precision.HIGHEST).astype(jnp.bfloat16)
    partial_value = jnp.dot(pair_embed, generator, preferred_element_type=jnp.float32)
    adapter_part = lax.psum_scatter(
        partial_value, "pair", scatter_dimension=1, tiled=True
    ).astype(jnp.bfloat16)
    flat_pairs = block_pair[:, 0]
    gen_major_pairs = flat_pairs.reshape(pair_count_axis, gen_count).T.reshape(-1)
    rows_per = quarter // adapter_rank
    outgoing = jnp.take(
        adapter_part.reshape(pair_count, rows_per, adapter_rank), gen_major_pairs, axis=0, mode="clip"
    )
    incoming = lax.all_to_all(outgoing, ("gen", "pair"), 0, 0, tiled=True)
    adapters = incoming.reshape(blocks_here, model_width, adapter_rank)
    token_blocks = tokens.reshape(blocks_here, BLK, model_width)
    cot_blocks = cotangent.reshape(blocks_here, BLK, adapter_rank)
    hidden = jnp.einsum("btd,bdr->btr", token_blocks, adapters, preferred_element_type=jnp.float32)
    logistic = jax.nn.sigmoid(hidden)
    grad_hidden = (
        cot_blocks.astype(jnp.float32) * logistic * (1.0 + hidden * (1.0 - logistic))
    ).astype(jnp.bfloat16)
    grad_tokens = (
        jnp.einsum("btr,bdr->btd", grad_hidden, adapters, preferred_element_type=jnp.float32)
        .astype(jnp.bfloat16)
        .reshape(tokens.shape)
    )
    outer_grads = jnp.einsum(
        "btd,btr->bdr", token_blocks, grad_hidden, preferred_element_type=jnp.float32
    )
    by_owner = outer_grads.reshape(gen_count * pair_count_axis, rows_per, adapter_rank).astype(jnp.bfloat16)
    returned = lax.all_to_all(by_owner, ("gen", "pair"), 0, 0, tiled=True)
    pair_ids = jnp.arange(pair_count, dtype=jnp.int32)
    segment_hot = (pair_ids[:, None] == gen_major_pairs[None, :]).astype(jnp.float32)
    row_grad = (
        jnp.einsum("pb,bxr->pxr", segment_hot, returned.astype(jnp.float32), precision=lax.Precision.HIGHEST)
        .astype(jnp.bfloat16)
        .reshape(pair_count, quarter)
    )
    grad_rounded = lax.all_gather(row_grad, "pair", axis=1, tiled=True)
    grad_generator = jnp.einsum(
        "pe,pc->ec", pair_embed, grad_rounded, preferred_element_type=jnp.float32
    ).astype(jnp.bfloat16)
    partial_pair = jnp.einsum(
        "pc,ec->pe", grad_rounded, generator, preferred_element_type=jnp.float32
    )
    grad_pair = partial_pair
    span = 1
    while span < gen_count:
        swap = [(i, i ^ span) for i in range(gen_count)]
        grad_pair = grad_pair + lax.ppermute(grad_pair, "gen", swap)
        span *= 2
    grad_embed = jnp.dot(hot_both.T, grad_pair, precision=lax.Precision.HIGHEST)
    return (grad_tokens, grad_generator, grad_embed)


def solution(mesh):
    placed = (
        P(("pair", "gen"), None),
        P(("pair", "gen"), None),
        P(),
        P(),
        P(),
        P(None, "pair"),
        P("pair", "gen"),
    )
    return jax.shard_map(
        shards,
        mesh=mesh,
        in_specs=placed,
        out_specs=(P(("pair", "gen"), None), P("pair", "gen"), P(None, "pair")),
        check_vma=False,
    )
```

```python
import jax
import jax.numpy as jnp
from jax import lax
from jax.sharding import PartitionSpec as P

BLK = 1024


def shards(tokens, cotangent, block_pair, src_lang, tgt_lang, lang_embed, generator):
    gen_count = lax.axis_size("gen")
    pair_count_axis = lax.axis_size("pair")
    blocks_here = tokens.shape[0] // BLK
    model_width = tokens.shape[1]
    adapter_rank = cotangent.shape[1]
    languages = lang_embed.shape[0]
    pair_count = src_lang.shape[0]
    chunk = generator.shape[1]
    quarter = chunk // pair_count_axis
    lang_ids = jnp.arange(languages, dtype=jnp.int32)
    hot_both = (src_lang[:, None] == lang_ids[None, :]).astype(jnp.float32) + (
        tgt_lang[:, None] == lang_ids[None, :]
    ).astype(jnp.float32)
    pair_embed = jnp.dot(hot_both, lang_embed, precision=lax.Precision.HIGHEST).astype(jnp.bfloat16)
    partial_value = jnp.dot(pair_embed, generator, preferred_element_type=jnp.float32)
    adapter_part = lax.psum_scatter(
        partial_value, "pair", scatter_dimension=1, tiled=True
    ).astype(jnp.bfloat16)
    flat_pairs = block_pair[:, 0]
    gen_major_pairs = flat_pairs.reshape(pair_count_axis, gen_count).T.reshape(-1)
    rows_per = quarter // adapter_rank
    outgoing = jnp.take(
        adapter_part.reshape(pair_count, rows_per, adapter_rank), gen_major_pairs, axis=0, mode="clip"
    )
    incoming = lax.all_to_all(outgoing, ("gen", "pair"), 0, 0, tiled=True)
    adapters = incoming.reshape(blocks_here, model_width, adapter_rank)
    token_blocks = tokens.reshape(blocks_here, BLK, model_width)
    cot_blocks = cotangent.reshape(blocks_here, BLK, adapter_rank)
    hidden = jnp.einsum("btd,bdr->btr", token_blocks, adapters, preferred_element_type=jnp.float32)
    logistic = jax.nn.sigmoid(hidden)
    grad_hidden = (
        cot_blocks.astype(jnp.float32) * logistic * (1.0 + hidden * (1.0 - logistic))
    ).astype(jnp.bfloat16)
    grad_tokens = (
        jnp.einsum("btr,bdr->btd", grad_hidden, adapters, preferred_element_type=jnp.float32)
        .astype(jnp.bfloat16)
        .reshape(tokens.shape)
    )
    outer_grads = jnp.einsum(
        "btd,btr->bdr", token_blocks, grad_hidden, preferred_element_type=jnp.float32
    )
    by_owner = outer_grads.reshape(gen_count * pair_count_axis, rows_per, adapter_rank).astype(jnp.bfloat16)
    returned = lax.all_to_all(by_owner, ("gen", "pair"), 0, 0, tiled=True)
    pair_ids = jnp.arange(pair_count, dtype=jnp.int32)
    segment_hot = (pair_ids[:, None] == gen_major_pairs[None, :]).astype(jnp.float32)
    row_grad = (
        jnp.einsum("pb,bxr->pxr", segment_hot, returned.astype(jnp.float32), precision=lax.Precision.HIGHEST)
        .astype(jnp.bfloat16)
        .reshape(pair_count, quarter)
    )
    grad_tokens, row_grad = lax.optimization_barrier((grad_tokens, row_grad))
    grad_rounded = lax.all_gather(row_grad, "pair", axis=1, tiled=True)
    grad_generator = jnp.einsum(
        "pe,pc->ec", pair_embed, grad_rounded, preferred_element_type=jnp.float32
    ).astype(jnp.bfloat16)
    partial_pair = jnp.einsum(
        "pc,ec->pe", grad_rounded, generator, preferred_element_type=jnp.float32
    )
    grad_pair = partial_pair
    span = 1
    while span < gen_count:
        swap = [(i, i ^ span) for i in range(gen_count)]
        grad_pair = grad_pair + lax.ppermute(grad_pair, "gen", swap)
        span *= 2
    grad_embed = jnp.dot(hot_both.T, grad_pair, precision=lax.Precision.HIGHEST)
    return (grad_tokens, grad_generator, grad_embed)


def solution(mesh):
    placed = (
        P(("pair", "gen"), None),
        P(("pair", "gen"), None),
        P(),
        P(),
        P(),
        P(None, "pair"),
        P("pair", "gen"),
    )
    return jax.shard_map(
        shards,
        mesh=mesh,
        in_specs=placed,
        out_specs=(P(("pair", "gen"), None), P("pair", "gen"), P(None, "pair")),
        check_vma=False,
    )
```

```python
import jax
import jax.numpy as jnp
from jax import lax
from jax.sharding import PartitionSpec as P
from jax.experimental import pallas as pl
from jax.experimental.pallas import tpu as pltpu

BLK = 1024
TAIL_COLS = 8192


def _tail_kernel(own_ref, embed_t_ref, grad_ref, gen_ref, *rest):
    out_ref, pair_ref = rest[-2], rest[-1]
    step = pl.program_id(0)
    grad_tile = grad_ref[...]
    out_ref[...] = jnp.dot(
        embed_t_ref[...], grad_tile, preferred_element_type=jnp.float32
    ).astype(out_ref.dtype)
    part = lax.dot_general(
        gen_ref[...], grad_tile, (((1,), (1,)), ((), ())), preferred_element_type=jnp.float32
    )

    @pl.when(step == 0)
    def _():
        pair_ref[...] = part

    @pl.when(step > 0)
    def _():
        pair_ref[...] += part


def grad_tail(own, embed_t, grads, generator, parts, previous=None):
    feats, cols = generator.shape
    pairs = grads.shape[0]
    quarter = cols // parts
    tile = min(TAIL_COLS, quarter)
    per_quarter = quarter // tile
    if previous is None:
        steps = per_quarter
        grad_map = lambda i, o: (0, i)
        col_map = lambda i, o: (0, o[0] * per_quarter + i)
        extra_specs, extra_args, aliases = [], [], {}
    else:
        steps = (parts - 1) * per_quarter

        def col_map(i, o):
            q = (o[0] + 1 + i // per_quarter) % parts
            return (0, q * per_quarter + i % per_quarter)

        grad_map = col_map
        extra_specs = [pl.BlockSpec(memory_space=pl.ANY)]
        extra_args = [previous]
        aliases = {4: 0}
    return pl.pallas_call(
        _tail_kernel,
        grid_spec=pltpu.PrefetchScalarGridSpec(
            num_scalar_prefetch=1,
            grid=(steps,),
            in_specs=[
                pl.BlockSpec((feats, pairs), lambda i, o: (0, 0)),
                pl.BlockSpec((pairs, tile), grad_map),
                pl.BlockSpec((feats, tile), col_map),
            ] + extra_specs,
            out_specs=[
                pl.BlockSpec((feats, tile), col_map),
                pl.BlockSpec((feats, pairs), lambda i, o: (0, 0)),
            ],
        ),
        out_shape=[
            jax.ShapeDtypeStruct((feats, cols), jnp.bfloat16),
            jax.ShapeDtypeStruct((feats, pairs), jnp.float32),
        ],
        input_output_aliases=aliases,
        compiler_params=pltpu.CompilerParams(dimension_semantics=("arbitrary",)),
    )(own, embed_t, grads, generator, *extra_args)


def shards(tokens, cotangent, block_pair, src_lang, tgt_lang, lang_embed, generator):
    gen_count = lax.axis_size("gen")
    pair_count_axis = lax.axis_size("pair")
    blocks_here = tokens.shape[0] // BLK
    model_width = tokens.shape[1]
    adapter_rank = cotangent.shape[1]
    languages = lang_embed.shape[0]
    pair_count = src_lang.shape[0]
    chunk = generator.shape[1]
    quarter = chunk // pair_count_axis
    lang_ids = jnp.arange(languages, dtype=jnp.int32)
    hot_both = (src_lang[:, None] == lang_ids[None, :]).astype(jnp.float32) + (
        tgt_lang[:, None] == lang_ids[None, :]
    ).astype(jnp.float32)
    pair_embed = jnp.dot(hot_both, lang_embed, precision=lax.Precision.HIGHEST).astype(jnp.bfloat16)
    partial_value = jnp.dot(pair_embed, generator, preferred_element_type=jnp.float32)
    adapter_part = lax.psum_scatter(
        partial_value, "pair", scatter_dimension=1, tiled=True
    ).astype(jnp.bfloat16)
    flat_pairs = block_pair[:, 0]
    gen_major_pairs = flat_pairs.reshape(pair_count_axis, gen_count).T.reshape(-1)
    rows_per = quarter // adapter_rank
    outgoing = jnp.take(
        adapter_part.reshape(pair_count, rows_per, adapter_rank), gen_major_pairs, axis=0, mode="clip"
    )
    incoming = lax.all_to_all(outgoing, ("gen", "pair"), 0, 0, tiled=True)
    adapters = incoming.reshape(blocks_here, model_width, adapter_rank)
    token_blocks = tokens.reshape(blocks_here, BLK, model_width)
    cot_blocks = cotangent.reshape(blocks_here, BLK, adapter_rank)
    hidden = jnp.einsum("btd,bdr->btr", token_blocks, adapters, preferred_element_type=jnp.float32)
    logistic = jax.nn.sigmoid(hidden)
    grad_hidden = (
        cot_blocks.astype(jnp.float32) * logistic * (1.0 + hidden * (1.0 - logistic))
    ).astype(jnp.bfloat16)
    grad_tokens = (
        jnp.einsum("btr,bdr->btd", grad_hidden, adapters, preferred_element_type=jnp.float32)
        .astype(jnp.bfloat16)
        .reshape(tokens.shape)
    )
    outer_grads = jnp.einsum(
        "btd,btr->bdr", token_blocks, grad_hidden, preferred_element_type=jnp.float32
    )
    by_owner = outer_grads.reshape(gen_count * pair_count_axis, rows_per, adapter_rank).astype(jnp.bfloat16)
    returned = lax.all_to_all(by_owner, ("gen", "pair"), 0, 0, tiled=True)
    pair_ids = jnp.arange(pair_count, dtype=jnp.int32)
    segment_hot = (pair_ids[:, None] == gen_major_pairs[None, :]).astype(jnp.float32)
    row_grad = (
        jnp.einsum("pb,bxr->pxr", segment_hot, returned.astype(jnp.float32), precision=lax.Precision.HIGHEST)
        .astype(jnp.bfloat16)
        .reshape(pair_count, quarter)
    )
    grad_tokens, row_grad = lax.optimization_barrier((grad_tokens, row_grad))
    grad_rounded = lax.all_gather(row_grad, "pair", axis=1, tiled=True)
    own = lax.axis_index("pair").astype(jnp.int32).reshape(1)
    embed_t = pair_embed.T
    first, own_part = grad_tail(own, embed_t, row_grad, generator, pair_count_axis)
    grad_generator, rest_part = grad_tail(own, embed_t, grad_rounded, generator, pair_count_axis, first)
    partial_pair = (own_part + rest_part).T
    grad_pair = partial_pair
    span = 1
    while span < gen_count:
        swap = [(i, i ^ span) for i in range(gen_count)]
        grad_pair = grad_pair + lax.ppermute(grad_pair, "gen", swap)
        span *= 2
    grad_embed = jnp.dot(hot_both.T, grad_pair, precision=lax.Precision.HIGHEST)
    return (grad_tokens, grad_generator, grad_embed)


def solution(mesh):
    placed = (
        P(("pair", "gen"), None),
        P(("pair", "gen"), None),
        P(),
        P(),
        P(),
        P(None, "pair"),
        P("pair", "gen"),
    )
    return jax.shard_map(
        shards,
        mesh=mesh,
        in_specs=placed,
        out_specs=(P(("pair", "gen"), None), P("pair", "gen"), P(None, "pair")),
        check_vma=False,
    )
```

```python
import jax
import jax.numpy as jnp
from jax import lax
from jax.sharding import PartitionSpec as P
from jax.experimental import pallas as pl
from jax.experimental.pallas import tpu as pltpu

BLK = 1024
TAIL_COLS = 8192


def _make_tail_kernel(do_gen, do_pair, aliased):
    def kernel(own_ref, *refs):
        refs = list(refs)
        embed_t_ref = refs.pop(0) if do_gen else None
        grad_ref = refs.pop(0)
        gen_ref = refs.pop(0) if do_pair else None
        if aliased:
            refs.pop(0)
        out_ref = refs.pop(0) if do_gen else None
        pair_ref = refs.pop(0) if do_pair else None
        grad_tile = grad_ref[...]
        if do_gen:
            out_ref[...] = jnp.dot(
                embed_t_ref[...], grad_tile, preferred_element_type=jnp.float32
            ).astype(out_ref.dtype)
        if do_pair:
            step = pl.program_id(0)
            part = lax.dot_general(
                gen_ref[...], grad_tile, (((1,), (1,)), ((), ())), preferred_element_type=jnp.float32
            )

            @pl.when(step == 0)
            def _():
                pair_ref[...] = part

            @pl.when(step > 0)
            def _():
                pair_ref[...] += part

    return kernel


def grad_tail(own, embed_t, grads, generator, parts, previous=None, do_gen=True, do_pair=True):
    feats, cols = generator.shape
    pairs = grads.shape[0]
    quarter = cols // parts
    tile = min(TAIL_COLS, quarter)
    per_quarter = quarter // tile
    if previous is None:
        steps = per_quarter
        grad_map = lambda i, o: (0, i)
        col_map = lambda i, o: (0, o[0] * per_quarter + i)
    else:
        steps = (parts - 1) * per_quarter

        def col_map(i, o):
            q = (o[0] + 1 + i // per_quarter) % parts
            return (0, q * per_quarter + i % per_quarter)

        grad_map = col_map
    in_specs, args, out_specs, out_shape = [], [], [], []
    if do_gen:
        in_specs.append(pl.BlockSpec((feats, pairs), lambda i, o: (0, 0)))
        args.append(embed_t)
    in_specs.append(pl.BlockSpec((pairs, tile), grad_map))
    args.append(grads)
    if do_pair:
        in_specs.append(pl.BlockSpec((feats, tile), col_map))
        args.append(generator)
    aliases = {}
    if previous is not None and do_gen:
        aliases = {len(args) + 1: 0}
        in_specs.append(pl.BlockSpec(memory_space=pl.ANY))
        args.append(previous)
    if do_gen:
        out_specs.append(pl.BlockSpec((feats, tile), col_map))
        out_shape.append(jax.ShapeDtypeStruct((feats, cols), jnp.bfloat16))
    if do_pair:
        out_specs.append(pl.BlockSpec((feats, pairs), lambda i, o: (0, 0)))
        out_shape.append(jax.ShapeDtypeStruct((feats, pairs), jnp.float32))
    return pl.pallas_call(
        _make_tail_kernel(do_gen, do_pair, bool(aliases)),
        grid_spec=pltpu.PrefetchScalarGridSpec(
            num_scalar_prefetch=1, grid=(steps,), in_specs=in_specs, out_specs=out_specs,
        ),
        out_shape=out_shape,
        input_output_aliases=aliases,
        compiler_params=pltpu.CompilerParams(dimension_semantics=("arbitrary",)),
    )(own, *args)


def shards(tokens, cotangent, block_pair, src_lang, tgt_lang, lang_embed, generator):
    gen_count = lax.axis_size("gen")
    pair_count_axis = lax.axis_size("pair")
    blocks_here = tokens.shape[0] // BLK
    model_width = tokens.shape[1]
    adapter_rank = cotangent.shape[1]
    languages = lang_embed.shape[0]
    pair_count = src_lang.shape[0]
    chunk = generator.shape[1]
    quarter = chunk // pair_count_axis
    lang_ids = jnp.arange(languages, dtype=jnp.int32)
    hot_both = (src_lang[:, None] == lang_ids[None, :]).astype(jnp.float32) + (
        tgt_lang[:, None] == lang_ids[None, :]
    ).astype(jnp.float32)
    pair_embed = jnp.dot(hot_both, lang_embed, precision=lax.Precision.HIGHEST).astype(jnp.bfloat16)
    partial_value = jnp.dot(pair_embed, generator, preferred_element_type=jnp.float32)
    adapter_part = lax.psum_scatter(
        partial_value, "pair", scatter_dimension=1, tiled=True
    ).astype(jnp.bfloat16)
    flat_pairs = block_pair[:, 0]
    gen_major_pairs = flat_pairs.reshape(pair_count_axis, gen_count).T.reshape(-1)
    rows_per = quarter // adapter_rank
    outgoing = jnp.take(
        adapter_part.reshape(pair_count, rows_per, adapter_rank), gen_major_pairs, axis=0, mode="clip"
    )
    incoming = lax.all_to_all(outgoing, ("gen", "pair"), 0, 0, tiled=True)
    adapters = incoming.reshape(blocks_here, model_width, adapter_rank)
    token_blocks = tokens.reshape(blocks_here, BLK, model_width)
    cot_blocks = cotangent.reshape(blocks_here, BLK, adapter_rank)
    hidden = jnp.einsum("btd,bdr->btr", token_blocks, adapters, preferred_element_type=jnp.float32)
    logistic = jax.nn.sigmoid(hidden)
    grad_hidden = (
        cot_blocks.astype(jnp.float32) * logistic * (1.0 + hidden * (1.0 - logistic))
    ).astype(jnp.bfloat16)
    grad_tokens = (
        jnp.einsum("btr,bdr->btd", grad_hidden, adapters, preferred_element_type=jnp.float32)
        .astype(jnp.bfloat16)
        .reshape(tokens.shape)
    )
    outer_grads = jnp.einsum(
        "btd,btr->bdr", token_blocks, grad_hidden, preferred_element_type=jnp.float32
    )
    by_owner = outer_grads.reshape(gen_count * pair_count_axis, rows_per, adapter_rank).astype(jnp.bfloat16)
    returned = lax.all_to_all(by_owner, ("gen", "pair"), 0, 0, tiled=True)
    pair_ids = jnp.arange(pair_count, dtype=jnp.int32)
    segment_hot = (pair_ids[:, None] == gen_major_pairs[None, :]).astype(jnp.float32)
    row_grad = (
        jnp.einsum("pb,bxr->pxr", segment_hot, returned.astype(jnp.float32), precision=lax.Precision.HIGHEST)
        .astype(jnp.bfloat16)
        .reshape(pair_count, quarter)
    )
    grad_tokens, row_grad = lax.optimization_barrier((grad_tokens, row_grad))
    grad_rounded = lax.all_gather(row_grad, "pair", axis=1, tiled=True)
    own = lax.axis_index("pair").astype(jnp.int32).reshape(1)
    embed_t = pair_embed.T
    first, own_part = grad_tail(own, embed_t, row_grad, generator, pair_count_axis)
    (rest_part,) = grad_tail(
        own, embed_t, grad_rounded, generator, pair_count_axis, first, do_gen=False
    )
    partial_pair = (own_part + rest_part).T
    grad_pair = partial_pair
    span = 1
    while span < gen_count:
        swap = [(i, i ^ span) for i in range(gen_count)]
        grad_pair = grad_pair + lax.ppermute(grad_pair, "gen", swap)
        span *= 2
    (grad_generator,) = grad_tail(
        own, embed_t, grad_rounded, generator, pair_count_axis, first, do_pair=False
    )
    grad_embed = jnp.dot(hot_both.T, grad_pair, precision=lax.Precision.HIGHEST)
    return (grad_tokens, grad_generator, grad_embed)


def solution(mesh):
    placed = (
        P(("pair", "gen"), None),
        P(("pair", "gen"), None),
        P(),
        P(),
        P(),
        P(None, "pair"),
        P("pair", "gen"),
    )
    return jax.shard_map(
        shards,
        mesh=mesh,
        in_specs=placed,
        out_specs=(P(("pair", "gen"), None), P("pair", "gen"), P(None, "pair")),
        check_vma=False,
    )
```

```python
import jax
import jax.numpy as jnp
from jax import lax
from jax.sharding import PartitionSpec as P
from jax.experimental import pallas as pl
from jax.experimental.pallas import tpu as pltpu

BLK = 1024
TAIL_COLS = 8192


def _tail_kernel(own_ref, embed_t_ref, grad_ref, gen_ref, *rest):
    out_ref, pair_ref = rest[-2], rest[-1]
    step = pl.program_id(0)
    grad_tile = grad_ref[...]
    out_ref[...] = jnp.dot(
        embed_t_ref[...], grad_tile, preferred_element_type=jnp.float32
    ).astype(out_ref.dtype)
    part = lax.dot_general(
        gen_ref[...], grad_tile, (((1,), (1,)), ((), ())), preferred_element_type=jnp.float32
    )

    @pl.when(step == 0)
    def _():
        pair_ref[...] = part

    @pl.when(step > 0)
    def _():
        pair_ref[...] += part


def grad_tail(own, embed_t, grads, generator, parts, previous=None):
    feats, cols = generator.shape
    pairs = grads.shape[0]
    quarter = cols // parts
    tile = min(TAIL_COLS, quarter)
    per_quarter = quarter // tile
    if previous is None:
        steps = per_quarter
        grad_map = lambda i, o: (0, i)
        col_map = lambda i, o: (0, o[0] * per_quarter + i)
        extra_specs, extra_args, aliases = [], [], {}
    else:
        steps = (parts - 1) * per_quarter

        def col_map(i, o):
            q = (o[0] + 1 + i // per_quarter) % parts
            return (0, q * per_quarter + i % per_quarter)

        grad_map = col_map
        extra_specs = [pl.BlockSpec(memory_space=pl.ANY)]
        extra_args = [previous]
        aliases = {4: 0}
    return pl.pallas_call(
        _tail_kernel,
        grid_spec=pltpu.PrefetchScalarGridSpec(
            num_scalar_prefetch=1,
            grid=(steps,),
            in_specs=[
                pl.BlockSpec((feats, pairs), lambda i, o: (0, 0)),
                pl.BlockSpec((pairs, tile), grad_map),
                pl.BlockSpec((feats, tile), col_map),
            ] + extra_specs,
            out_specs=[
                pl.BlockSpec((feats, tile), col_map),
                pl.BlockSpec((feats, pairs), lambda i, o: (0, 0)),
            ],
        ),
        out_shape=[
            jax.ShapeDtypeStruct((feats, cols), jnp.bfloat16),
            jax.ShapeDtypeStruct((feats, pairs), jnp.float32),
        ],
        input_output_aliases=aliases,
        compiler_params=pltpu.CompilerParams(dimension_semantics=("arbitrary",)),
    )(own, embed_t, grads, generator, *extra_args)


def shards(tokens, cotangent, block_pair, src_lang, tgt_lang, lang_embed, generator):
    gen_count = lax.axis_size("gen")
    pair_count_axis = lax.axis_size("pair")
    blocks_here = tokens.shape[0] // BLK
    model_width = tokens.shape[1]
    adapter_rank = cotangent.shape[1]
    languages = lang_embed.shape[0]
    pair_count = src_lang.shape[0]
    chunk = generator.shape[1]
    quarter = chunk // pair_count_axis
    lang_ids = jnp.arange(languages, dtype=jnp.int32)
    hot_both = (src_lang[:, None] == lang_ids[None, :]).astype(jnp.float32) + (
        tgt_lang[:, None] == lang_ids[None, :]
    ).astype(jnp.float32)
    pair_embed = jnp.dot(hot_both, lang_embed, precision=lax.Precision.HIGHEST).astype(jnp.bfloat16)
    partial_value = jnp.dot(pair_embed, generator, preferred_element_type=jnp.float32)
    adapter_part = lax.psum_scatter(
        partial_value, "pair", scatter_dimension=1, tiled=True
    ).astype(jnp.bfloat16)
    flat_pairs = block_pair[:, 0]
    gen_major_pairs = flat_pairs.reshape(pair_count_axis, gen_count).T.reshape(-1)
    rows_per = quarter // adapter_rank
    outgoing = jnp.take(
        adapter_part.reshape(pair_count, rows_per, adapter_rank), gen_major_pairs, axis=0, mode="clip"
    )
    incoming = lax.all_to_all(outgoing, ("gen", "pair"), 0, 0, tiled=True)
    adapters = incoming.reshape(blocks_here, model_width, adapter_rank)
    token_blocks = tokens.reshape(blocks_here, BLK, model_width)
    cot_blocks = cotangent.reshape(blocks_here, BLK, adapter_rank)
    hidden = jnp.einsum("btd,bdr->btr", token_blocks, adapters, preferred_element_type=jnp.float32)
    logistic = jax.nn.sigmoid(hidden)
    grad_hidden = (
        cot_blocks.astype(jnp.float32) * logistic * (1.0 + hidden * (1.0 - logistic))
    ).astype(jnp.bfloat16)
    grad_tokens = (
        jnp.einsum("btr,bdr->btd", grad_hidden, adapters, preferred_element_type=jnp.float32)
        .astype(jnp.bfloat16)
        .reshape(tokens.shape)
    )
    outer_grads = jnp.einsum(
        "btd,btr->bdr", token_blocks, grad_hidden, preferred_element_type=jnp.float32
    )
    by_owner = outer_grads.reshape(gen_count * pair_count_axis, rows_per, adapter_rank).astype(jnp.bfloat16)
    returned = lax.all_to_all(by_owner, ("gen", "pair"), 0, 0, tiled=True)
    pair_ids = jnp.arange(pair_count, dtype=jnp.int32)
    segment_hot = (pair_ids[:, None] == gen_major_pairs[None, :]).astype(jnp.float32)
    row_grad = (
        jnp.dot(
            segment_hot.astype(jnp.bfloat16), returned.reshape(pair_count_axis * gen_count, quarter),
            preferred_element_type=jnp.float32,
        ).astype(jnp.bfloat16)
    )
    grad_tokens, row_grad = lax.optimization_barrier((grad_tokens, row_grad))
    grad_rounded = lax.all_gather(row_grad, "pair", axis=1, tiled=True)
    own = lax.axis_index("pair").astype(jnp.int32).reshape(1)
    embed_t = pair_embed.T
    first, own_part = grad_tail(own, embed_t, row_grad, generator, pair_count_axis)
    grad_generator, rest_part = grad_tail(own, embed_t, grad_rounded, generator, pair_count_axis, first)
    partial_pair = (own_part + rest_part).T
    grad_pair = partial_pair
    span = 1
    while span < gen_count:
        swap = [(i, i ^ span) for i in range(gen_count)]
        grad_pair = grad_pair + lax.ppermute(grad_pair, "gen", swap)
        span *= 2
    grad_embed = jnp.dot(hot_both.T, grad_pair, precision=lax.Precision.HIGHEST)
    return (grad_tokens, grad_generator, grad_embed)


def solution(mesh):
    placed = (
        P(("pair", "gen"), None),
        P(("pair", "gen"), None),
        P(),
        P(),
        P(),
        P(None, "pair"),
        P("pair", "gen"),
    )
    return jax.shard_map(
        shards,
        mesh=mesh,
        in_specs=placed,
        out_specs=(P(("pair", "gen"), None), P("pair", "gen"), P(None, "pair")),
        check_vma=False,
    )
```

```python
import jax
import jax.numpy as jnp
from jax import lax
from jax.sharding import PartitionSpec as P
from jax.experimental import pallas as pl
from jax.experimental.pallas import tpu as pltpu

BLK = 1024
TAIL_COLS = 8192


def _tail_kernel(own_ref, embed_t_ref, grad_ref, gen_ref, *rest):
    out_ref, pair_ref = rest[-2], rest[-1]
    step = pl.program_id(0)
    grad_tile = grad_ref[...]
    out_ref[...] = jnp.dot(
        embed_t_ref[...], grad_tile, preferred_element_type=jnp.float32
    ).astype(out_ref.dtype)
    part = lax.dot_general(
        gen_ref[...], grad_tile, (((1,), (1,)), ((), ())), preferred_element_type=jnp.float32
    )

    @pl.when(step == 0)
    def _():
        pair_ref[...] = part

    @pl.when(step > 0)
    def _():
        pair_ref[...] += part


def grad_tail(own, embed_t, grads, generator, parts, previous=None):
    feats, cols = generator.shape
    pairs = grads.shape[0]
    quarter = cols // parts
    tile = min(TAIL_COLS, quarter)
    per_quarter = quarter // tile
    if previous is None:
        steps = per_quarter
        grad_map = lambda i, o: (0, i)
        col_map = lambda i, o: (0, o[0] * per_quarter + i)
        extra_specs, extra_args, aliases = [], [], {}
    else:
        steps = (parts - 1) * per_quarter

        def col_map(i, o):
            q = (o[0] + 1 + i // per_quarter) % parts
            return (0, q * per_quarter + i % per_quarter)

        grad_map = col_map
        extra_specs = [pl.BlockSpec(memory_space=pl.ANY)]
        extra_args = [previous]
        aliases = {4: 0}
    return pl.pallas_call(
        _tail_kernel,
        grid_spec=pltpu.PrefetchScalarGridSpec(
            num_scalar_prefetch=1,
            grid=(steps,),
            in_specs=[
                pl.BlockSpec((feats, pairs), lambda i, o: (0, 0)),
                pl.BlockSpec((pairs, tile), grad_map),
                pl.BlockSpec((feats, tile), col_map),
            ] + extra_specs,
            out_specs=[
                pl.BlockSpec((feats, tile), col_map),
                pl.BlockSpec((feats, pairs), lambda i, o: (0, 0)),
            ],
        ),
        out_shape=[
            jax.ShapeDtypeStruct((feats, cols), jnp.bfloat16),
            jax.ShapeDtypeStruct((feats, pairs), jnp.float32),
        ],
        input_output_aliases=aliases,
        compiler_params=pltpu.CompilerParams(dimension_semantics=("arbitrary",)),
    )(own, embed_t, grads, generator, *extra_args)


def shards(tokens, cotangent, block_pair, src_lang, tgt_lang, lang_embed, generator):
    gen_count = lax.axis_size("gen")
    pair_count_axis = lax.axis_size("pair")
    blocks_here = tokens.shape[0] // BLK
    model_width = tokens.shape[1]
    adapter_rank = cotangent.shape[1]
    languages = lang_embed.shape[0]
    pair_count = src_lang.shape[0]
    chunk = generator.shape[1]
    quarter = chunk // pair_count_axis
    lang_ids = jnp.arange(languages, dtype=jnp.int32)
    hot_both = (src_lang[:, None] == lang_ids[None, :]).astype(jnp.float32) + (
        tgt_lang[:, None] == lang_ids[None, :]
    ).astype(jnp.float32)
    pair_embed = jnp.dot(hot_both, lang_embed, precision=lax.Precision.HIGHEST).astype(jnp.bfloat16)
    partial_value = jnp.dot(pair_embed, generator, preferred_element_type=jnp.float32)
    adapter_part = lax.psum_scatter(
        partial_value, "pair", scatter_dimension=1, tiled=True
    )
    flat_pairs = block_pair[:, 0]
    gen_major_pairs = flat_pairs.reshape(pair_count_axis, gen_count).T.reshape(-1)
    rows_per = quarter // adapter_rank
    outgoing = jnp.take(
        adapter_part.reshape(pair_count, rows_per, adapter_rank), gen_major_pairs, axis=0, mode="clip"
    ).astype(jnp.bfloat16)
    incoming = lax.all_to_all(outgoing, ("gen", "pair"), 0, 0, tiled=True)
    adapters = incoming.reshape(blocks_here, model_width, adapter_rank)
    token_blocks = tokens.reshape(blocks_here, BLK, model_width)
    cot_blocks = cotangent.reshape(blocks_here, BLK, adapter_rank)
    hidden = jnp.einsum("btd,bdr->btr", token_blocks, adapters, preferred_element_type=jnp.float32)
    logistic = jax.nn.sigmoid(hidden)
    grad_hidden = (
        cot_blocks.astype(jnp.float32) * logistic * (1.0 + hidden * (1.0 - logistic))
    ).astype(jnp.bfloat16)
    grad_tokens = (
        jnp.einsum("btr,bdr->btd", grad_hidden, adapters, preferred_element_type=jnp.float32)
        .astype(jnp.bfloat16)
        .reshape(tokens.shape)
    )
    outer_grads = jnp.einsum(
        "btd,btr->bdr", token_blocks, grad_hidden, preferred_element_type=jnp.float32
    )
    by_owner = outer_grads.reshape(gen_count * pair_count_axis, rows_per, adapter_rank).astype(jnp.bfloat16)
    returned = lax.all_to_all(by_owner, ("gen", "pair"), 0, 0, tiled=True)
    pair_ids = jnp.arange(pair_count, dtype=jnp.int32)
    segment_hot = (pair_ids[:, None] == gen_major_pairs[None, :]).astype(jnp.float32)
    row_grad = (
        jnp.dot(
            segment_hot.astype(jnp.bfloat16), returned.reshape(pair_count_axis * gen_count, quarter),
            preferred_element_type=jnp.float32,
        ).astype(jnp.bfloat16)
    )
    grad_tokens, row_grad = lax.optimization_barrier((grad_tokens, row_grad))
    grad_rounded = lax.all_gather(row_grad, "pair", axis=1, tiled=True)
    own = lax.axis_index("pair").astype(jnp.int32).reshape(1)
    embed_t = pair_embed.T
    first, own_part = grad_tail(own, embed_t, row_grad, generator, pair_count_axis)
    grad_generator, rest_part = grad_tail(own, embed_t, grad_rounded, generator, pair_count_axis, first)
    partial_pair = (own_part + rest_part).T
    grad_pair = partial_pair
    span = 1
    while span < gen_count:
        swap = [(i, i ^ span) for i in range(gen_count)]
        grad_pair = grad_pair + lax.ppermute(grad_pair, "gen", swap)
        span *= 2
    grad_embed = jnp.dot(hot_both.T, grad_pair, precision=lax.Precision.HIGHEST)
    return (grad_tokens, grad_generator, grad_embed)


def solution(mesh):
    placed = (
        P(("pair", "gen"), None),
        P(("pair", "gen"), None),
        P(),
        P(),
        P(),
        P(None, "pair"),
        P("pair", "gen"),
    )
    return jax.shard_map(
        shards,
        mesh=mesh,
        in_specs=placed,
        out_specs=(P(("pair", "gen"), None), P("pair", "gen"), P(None, "pair")),
        check_vma=False,
    )
```

```python
import jax
import jax.numpy as jnp
from jax import lax
from jax.sharding import PartitionSpec as P
from jax.experimental import pallas as pl
from jax.experimental.pallas import tpu as pltpu

BLK = 1024
TAIL_COLS = 16384


def _tail_kernel(own_ref, embed_t_ref, grad_ref, gen_ref, *rest):
    out_ref, pair_ref = rest[-2], rest[-1]
    step = pl.program_id(0)
    grad_tile = grad_ref[...]
    out_ref[...] = jnp.dot(
        embed_t_ref[...], grad_tile, preferred_element_type=jnp.float32
    ).astype(out_ref.dtype)
    part = lax.dot_general(
        gen_ref[...], grad_tile, (((1,), (1,)), ((), ())), preferred_element_type=jnp.float32
    )

    @pl.when(step == 0)
    def _():
        pair_ref[...] = part

    @pl.when(step > 0)
    def _():
        pair_ref[...] += part


def grad_tail(own, embed_t, grads, generator, parts, previous=None):
    feats, cols = generator.shape
    pairs = grads.shape[0]
    quarter = cols // parts
    tile = min(TAIL_COLS, quarter)
    per_quarter = quarter // tile
    if previous is None:
        steps = per_quarter
        grad_map = lambda i, o: (0, i)
        col_map = lambda i, o: (0, o[0] * per_quarter + i)
        extra_specs, extra_args, aliases = [], [], {}
    else:
        steps = (parts - 1) * per_quarter

        def col_map(i, o):
            q = (o[0] + 1 + i // per_quarter) % parts
            return (0, q * per_quarter + i % per_quarter)

        grad_map = col_map
        extra_specs = [pl.BlockSpec(memory_space=pl.ANY)]
        extra_args = [previous]
        aliases = {4: 0}
    return pl.pallas_call(
        _tail_kernel,
        grid_spec=pltpu.PrefetchScalarGridSpec(
            num_scalar_prefetch=1,
            grid=(steps,),
            in_specs=[
                pl.BlockSpec((feats, pairs), lambda i, o: (0, 0)),
                pl.BlockSpec((pairs, tile), grad_map),
                pl.BlockSpec((feats, tile), col_map),
            ] + extra_specs,
            out_specs=[
                pl.BlockSpec((feats, tile), col_map),
                pl.BlockSpec((feats, pairs), lambda i, o: (0, 0)),
            ],
        ),
        out_shape=[
            jax.ShapeDtypeStruct((feats, cols), jnp.bfloat16),
            jax.ShapeDtypeStruct((feats, pairs), jnp.float32),
        ],
        input_output_aliases=aliases,
        compiler_params=pltpu.CompilerParams(dimension_semantics=("arbitrary",)),
    )(own, embed_t, grads, generator, *extra_args)


def shards(tokens, cotangent, block_pair, src_lang, tgt_lang, lang_embed, generator):
    gen_count = lax.axis_size("gen")
    pair_count_axis = lax.axis_size("pair")
    blocks_here = tokens.shape[0] // BLK
    model_width = tokens.shape[1]
    adapter_rank = cotangent.shape[1]
    languages = lang_embed.shape[0]
    pair_count = src_lang.shape[0]
    chunk = generator.shape[1]
    quarter = chunk // pair_count_axis
    lang_ids = jnp.arange(languages, dtype=jnp.int32)
    hot_both = (src_lang[:, None] == lang_ids[None, :]).astype(jnp.float32) + (
        tgt_lang[:, None] == lang_ids[None, :]
    ).astype(jnp.float32)
    pair_embed = jnp.dot(hot_both, lang_embed, precision=lax.Precision.HIGHEST).astype(jnp.bfloat16)
    partial_value = jnp.dot(pair_embed, generator, preferred_element_type=jnp.float32)
    adapter_part = lax.psum_scatter(
        partial_value, "pair", scatter_dimension=1, tiled=True
    ).astype(jnp.bfloat16)
    flat_pairs = block_pair[:, 0]
    gen_major_pairs = flat_pairs.reshape(pair_count_axis, gen_count).T.reshape(-1)
    rows_per = quarter // adapter_rank
    outgoing = jnp.take(
        adapter_part.reshape(pair_count, rows_per, adapter_rank), gen_major_pairs, axis=0, mode="clip"
    )
    incoming = lax.all_to_all(outgoing, ("gen", "pair"), 0, 0, tiled=True)
    adapters = incoming.reshape(blocks_here, model_width, adapter_rank)
    token_blocks = tokens.reshape(blocks_here, BLK, model_width)
    cot_blocks = cotangent.reshape(blocks_here, BLK, adapter_rank)
    hidden = jnp.einsum("btd,bdr->btr", token_blocks, adapters, preferred_element_type=jnp.float32)
    logistic = jax.nn.sigmoid(hidden)
    grad_hidden = (
        cot_blocks.astype(jnp.float32) * logistic * (1.0 + hidden * (1.0 - logistic))
    ).astype(jnp.bfloat16)
    grad_tokens = (
        jnp.einsum("btr,bdr->btd", grad_hidden, adapters, preferred_element_type=jnp.float32)
        .astype(jnp.bfloat16)
        .reshape(tokens.shape)
    )
    outer_grads = jnp.einsum(
        "btd,btr->bdr", token_blocks, grad_hidden, preferred_element_type=jnp.float32
    )
    by_owner = outer_grads.reshape(gen_count * pair_count_axis, rows_per, adapter_rank).astype(jnp.bfloat16)
    returned = lax.all_to_all(by_owner, ("gen", "pair"), 0, 0, tiled=True)
    pair_ids = jnp.arange(pair_count, dtype=jnp.int32)
    segment_hot = (pair_ids[:, None] == gen_major_pairs[None, :]).astype(jnp.float32)
    row_grad = (
        jnp.dot(
            segment_hot.astype(jnp.bfloat16), returned.reshape(pair_count_axis * gen_count, quarter),
            preferred_element_type=jnp.float32,
        ).astype(jnp.bfloat16)
    )
    grad_tokens, row_grad = lax.optimization_barrier((grad_tokens, row_grad))
    grad_rounded = lax.all_gather(row_grad, "pair", axis=1, tiled=True)
    own = lax.axis_index("pair").astype(jnp.int32).reshape(1)
    embed_t = pair_embed.T
    first, own_part = grad_tail(own, embed_t, row_grad, generator, pair_count_axis)
    grad_generator, rest_part = grad_tail(own, embed_t, grad_rounded, generator, pair_count_axis, first)
    partial_pair = (own_part + rest_part).T
    grad_pair = partial_pair
    span = 1
    while span < gen_count:
        swap = [(i, i ^ span) for i in range(gen_count)]
        grad_pair = grad_pair + lax.ppermute(grad_pair, "gen", swap)
        span *= 2
    grad_embed = jnp.dot(hot_both.T, grad_pair, precision=lax.Precision.HIGHEST)
    return (grad_tokens, grad_generator, grad_embed)


def solution(mesh):
    placed = (
        P(("pair", "gen"), None),
        P(("pair", "gen"), None),
        P(),
        P(),
        P(),
        P(None, "pair"),
        P("pair", "gen"),
    )
    return jax.shard_map(
        shards,
        mesh=mesh,
        in_specs=placed,
        out_specs=(P(("pair", "gen"), None), P("pair", "gen"), P(None, "pair")),
        check_vma=False,
    )
```
